32 devices in a mesh: occ: 4 (over z), vir: 8 (over y, x, core).
Axes of the slice: x: 2, y: 2, z: 4, core: 2. Of those that a mesh axis runs over, the one named last changes fastest.
Arguments:
- lam: bfloat16 [4096, 12288], P('occ', 'vir'), may hold values from -6 to 6
- integrals: bfloat16 [12288, 1024], P('vir', 'occ'), may hold values from -0.21875 to 0.21875
- occ_sym: int32 [32], P('occ'), may hold values from 0 to 7, as said below
- cd_sym: int32 [96], P('vir'), may hold values from 0 to 7
- ab_sym: int32 [8], replicated, may hold values from 0 to 7
Outputs:
- ladder: bfloat16 [4096, 1024], P('occ', 'vir')
The draws below stay inside these ranges and needn't reach their ends.
Inputs may be any that keep to these rules, and one draw needn't show every extreme that they name: `occ_sym`: in each aligned block of 8 tiles (those of one index of occ) each representation labels the same number of tiles, 1 of them.
All inputs are finite; a program needn't handle non-finite values.
Results may differ from the reference program's by a relative error of at most 0.001.
Values may be sent and summed in bfloat16 or wider, within the bound.
No kernel may reach another device: no remote copies, remote signals or barrier semaphores. Data moves between devices by JAX's collectives and lax.ppermute only.
A program may use at most 128 MiB of HBM per device.

```python
import math
import jax
import jax.numpy as jnp
import numpy as np

TB = 128
NIRREP = 8
OT_DEV = 8
OCC_TILES = 32
CD_TILES = 96
COL_TILES = 8


def draw_occ_sym(key, part):
    block_keys = jax.random.split(key, OCC_TILES // OT_DEV)
    labels = jnp.arange(OT_DEV, dtype=jnp.int32) % NIRREP
    shuffled = jax.vmap(lambda one_key: jax.random.permutation(one_key, labels))(block_keys)
    return shuffled.reshape(-1).astype(jnp.int32)


def set_ends(result, rng, smallest, largest):
    index_at = [jax.random.randint(jax.random.fold_in(rng, axis), (), 0, length) for axis, length in enumerate(result.shape)]
    widest = result.shape.index(max(result.shape))
    neighbour = index_at[:widest] + [(index_at[widest] + 1) % result.shape[widest]] + index_at[widest + 1:]
    return result.at[tuple(index_at)].set(smallest).at[tuple(neighbour)].set(largest)


def raised(array, own_key, source, target, blocks, factor):
    owner, partner = [(jnp.arange(array.shape[axis_at]) // (array.shape[axis_at] // blocks)).reshape([-1 if axis == axis_at else 1 for axis in range(array.ndim)]) for axis_at in (source, target)]
    chosen = jax.random.permutation(own_key, blocks)[partner]
    strong = (owner == chosen) | (owner == (partner + blocks // 2) % blocks)
    return jnp.where(strong, factor * array, array)


def levels(own_key, shape, pieces, least, largest):
    def one(position, shards_of):
        heights = jax.random.uniform(jax.random.fold_in(jax.random.fold_in(own_key, 6), position), (shards_of,), jnp.float32, least / len(pieces), largest / len(pieces))
        return jnp.repeat(jnp.exp(heights), shape[position] // shards_of).reshape((-1,) + (1,) * (len(shape) - position - 1))

    loudness = one(*pieces[0])
    for cut in pieces[1:]:
        loudness = loudness * one(*cut)
    return loudness


def rank_bounds(amount, slope):
    weights = [(1 << 20) // math.isqrt(standing ** slope) + 1 for standing in range(1, amount + 1)]
    deviation = 1 + sum(weights) // (1 << 30)
    return np.cumsum(np.array([max(1, weight // deviation) for weight in weights]))


def ranked_ids(own_key, dims, number_of, skew):
    grid = rank_bounds(number_of, skew)
    lot = jax.random.randint(jax.random.fold_in(own_key, 1), dims, 0, int(grid[number_of - 1]))
    grade = jnp.searchsorted(jnp.asarray(grid, jnp.int32), lot, side="right")
    return jax.random.permutation(jax.random.fold_in(own_key, 2), number_of)[grade].astype(jnp.int32)


def bell_draw(own_key, extent, deviation, limit, cuts=(), kind=jnp.bfloat16):
    gain = levels(own_key, extent, cuts, -0.22, 0.18) if cuts else 1.0
    values = jax.random.normal(own_key, extent, jnp.float32) * deviation * gain
    return jnp.minimum(jnp.maximum(values, -limit), limit).astype(kind)


def heavy_noise(key, dims, scale, limit, shards, heavy, kind=jnp.bfloat16):
    values = scale * jax.random.normal(key, dims, jnp.float32)
    if shards:
        values = values * levels(key, dims, shards, -0.22, 0.18)
    return jnp.clip(raised(values, jax.random.fold_in(key, 3), *heavy), -limit, limit).astype(kind)


def setup_inputs(seed: int = 0) -> dict:
    arg_keys = jax.random.split(jax.random.key(seed), 6)
    return {
        "lam": bell_draw(arg_keys[0], (OCC_TILES * TB, CD_TILES * TB), 1.0, 6.0, ((0, 4), (1, 8))),
        "integrals": heavy_noise(arg_keys[1], (CD_TILES * TB, COL_TILES * TB), (CD_TILES * TB // NIRREP) ** -0.5, 0.21875, ((0, 8), (1, 4)), (0, 1, 8, 2.0)),
        "occ_sym": draw_occ_sym(jax.random.fold_in(arg_keys[5], 71), 0),
        "cd_sym": set_ends(ranked_ids(arg_keys[3], (CD_TILES,), NIRREP, 1), jax.random.fold_in(arg_keys[3], 3), 0, NIRREP - 1).astype(jnp.int32),
        "ab_sym": set_ends(jax.random.randint(arg_keys[4], (COL_TILES,), 0, NIRREP), jax.random.fold_in(arg_keys[4], 1), 0, NIRREP - 1).astype(jnp.int32),
    }


def reference(lam, integrals, occ_sym, cd_sym, ab_sym):
    lam_mask = (occ_sym[:, None] == cd_sym[None, :]).astype(jnp.bfloat16)
    lam_kept = (lam.reshape(OCC_TILES, TB, CD_TILES, TB) * lam_mask[:, None, :, None]).reshape(OCC_TILES * TB, CD_TILES * TB)
    int_mask = (cd_sym[:, None] == ab_sym[None, :]).astype(jnp.bfloat16)
    int_kept = (integrals.reshape(CD_TILES, TB, COL_TILES, TB) * int_mask[:, None, :, None]).reshape(CD_TILES * TB, COL_TILES * TB)
    return jnp.dot(lam_kept, int_kept, preferred_element_type=jnp.float32).astype(jnp.bfloat16)
```

```python
import jax
import jax.numpy as jnp
from jax import lax
from jax.sharding import PartitionSpec as P


def on_device(lam, integrals, occ_sym, cd_sym, ab_sym):
    row_tiles = occ_sym.shape[0]
    cd_tiles = cd_sym.shape[0]
    tile_edge = lam.shape[0] // row_tiles
    col_tiles = ab_sym.shape[0]
    own_cols = integrals.shape[1] // tile_edge
    row_of = jnp.argmax(occ_sym[None, :] == ab_sym[:, None], axis=1)
    own_sym = lax.dynamic_slice_in_dim(ab_sym, lax.axis_index("occ") * own_cols, own_cols)
    int_mask = (cd_sym[:, None] == own_sym[None, :]).astype(jnp.bfloat16)
    int_kept = (
        integrals.reshape(cd_tiles, tile_edge, own_cols, tile_edge) * int_mask[:, None, :, None]
    ).reshape(integrals.shape)
    int_all = lax.all_gather(int_kept, "occ", axis=1, tiled=True)
    int_cols = int_all.reshape(cd_tiles * tile_edge, col_tiles, tile_edge)
    lam_rows = lam.reshape(row_tiles, tile_edge, cd_tiles * tile_edge)[row_of]
    partial_sum = jnp.einsum(
        "trk,ktc->rtc", lam_rows, int_cols, preferred_element_type=jnp.float32
    ).reshape(tile_edge, col_tiles * tile_edge)
    summed = lax.psum_scatter(partial_sum, "vir", scatter_dimension=1, tiled=True)
    own_row = row_of[lax.axis_index("vir")]
    keep = (jnp.arange(row_tiles) == own_row)[:, None, None]
    out = jnp.where(keep, summed.astype(jnp.bfloat16)[None], jnp.zeros((), jnp.bfloat16))
    return out.reshape(row_tiles * tile_edge, summed.shape[1])


def solution(mesh):
    in_specs = (P("occ", "vir"), P("vir", "occ"), P("occ"), P("vir"), P())
    out_specs = P("occ", "vir")
    return jax.shard_map(
        on_device, mesh=mesh, in_specs=in_specs, out_specs=out_specs, check_vma=False
    )
```

```python
import jax
import jax.numpy as jnp
from jax import lax
from jax.sharding import PartitionSpec as P


def halving_reduce_scatter(parts, axis):
    n = lax.axis_size(axis)
    me = lax.axis_index(axis)
    step = 1
    while step < n:
        bit = (me // step) % 2
        pairs = parts.reshape(parts.shape[0] // 2, 2, *parts.shape[1:])
        keep = lax.dynamic_index_in_dim(pairs, bit, axis=1, keepdims=False)
        send = lax.dynamic_index_in_dim(pairs, 1 - bit, axis=1, keepdims=False)
        perm = [(j, j ^ step) for j in range(n)]
        parts = keep + lax.ppermute(send, axis, perm)
        step *= 2
    return parts[0]


def on_device(lam, integrals, occ_sym, cd_sym, ab_sym):
    row_tiles = occ_sym.shape[0]
    cd_tiles = cd_sym.shape[0]
    tile_edge = lam.shape[0] // row_tiles
    col_tiles = ab_sym.shape[0]
    own_cols = integrals.shape[1] // tile_edge
    row_of = jnp.argmax(occ_sym[None, :] == ab_sym[:, None], axis=1)
    own_sym = lax.dynamic_slice_in_dim(ab_sym, lax.axis_index("occ") * own_cols, own_cols)
    int_mask = (cd_sym[:, None] == own_sym[None, :]).astype(jnp.bfloat16)
    int_kept = (
        integrals.reshape(cd_tiles, tile_edge, own_cols, tile_edge) * int_mask[:, None, :, None]
    ).reshape(integrals.shape)
    int_all = lax.all_gather(int_kept, "occ", axis=1, tiled=True)
    int_cols = int_all.reshape(cd_tiles * tile_edge, col_tiles, tile_edge)
    lam_rows = lam.reshape(row_tiles, tile_edge, cd_tiles * tile_edge)[row_of]
    partial_sum = jnp.einsum(
        "trk,ktc->trc", lam_rows, int_cols, preferred_element_type=jnp.float32
    )
    summed = halving_reduce_scatter(partial_sum, "vir")
    own_row = row_of[lax.axis_index("vir")]
    keep = (jnp.arange(row_tiles) == own_row)[:, None, None]
    out = jnp.where(keep, summed.astype(jnp.bfloat16)[None], jnp.zeros((), jnp.bfloat16))
    return out.reshape(row_tiles * tile_edge, summed.shape[1])


def solution(mesh):
    in_specs = (P("occ", "vir"), P("vir", "occ"), P("occ"), P("vir"), P())
    out_specs = P("occ", "vir")
    return jax.shard_map(
        on_device, mesh=mesh, in_specs=in_specs, out_specs=out_specs, check_vma=False
    )
```

```python
import jax
import jax.numpy as jnp
from jax import lax
from jax.sharding import PartitionSpec as P


def halving_reduce_scatter(parts, axis):
    n = lax.axis_size(axis)
    me = lax.axis_index(axis)
    step = 1
    while step < n:
        bit = (me // step) % 2
        pairs = parts.reshape(parts.shape[0] // 2, 2, *parts.shape[1:])
        keep = lax.dynamic_index_in_dim(pairs, bit, axis=1, keepdims=False)
        send = lax.dynamic_index_in_dim(pairs, 1 - bit, axis=1, keepdims=False)
        perm = [(j, j ^ step) for j in range(n)]
        parts = keep + lax.ppermute(send, axis, perm)
        step *= 2
    return parts[0]


def doubling_max(value, axis):
    n = lax.axis_size(axis)
    step = 1
    while step < n:
        value = jnp.maximum(value, lax.ppermute(value, axis, [(j, j ^ step) for j in range(n)]))
        step *= 2
    return value


def tiles_at(array, rows, cols, edge):
    take = lambda r, c: lax.dynamic_slice(array, (r * edge, c * edge), (edge, edge))
    return jax.vmap(take)(rows, cols)


def packed_partials(lam, integrals, kept, row_of, cap, edge):
    peers, cd_tiles, own_cols = kept.shape
    col_tiles = peers * own_cols
    flat = kept.reshape(peers, cd_tiles * own_cols)
    rank = jnp.cumsum(flat, axis=1) - 1
    hit = flat[:, None, :] & (rank[:, None, :] == jnp.arange(cap)[None, :, None])
    order = jnp.sum(hit * jnp.arange(cd_tiles * own_cols), axis=2)
    valid = jnp.any(hit, axis=2)
    q = order // own_cols
    c = order % own_cols
    me = lax.axis_index("occ")
    sent = tiles_at(integrals, q[me], c[me], edge)
    received = lax.all_gather(sent, "occ", axis=0, tiled=True)
    t = (jnp.arange(peers)[:, None] * own_cols + c).reshape(-1)
    valid = valid.reshape(-1)
    lam_tiles = tiles_at(lam, row_of[t], q.reshape(-1), edge)
    lam_tiles = jnp.where(valid[:, None, None], lam_tiles, jnp.zeros((), lam.dtype))
    products = jnp.einsum(
        "srm,smc->src", lam_tiles, received, preferred_element_type=jnp.float32
    )
    owner = (t[None, :] == jnp.arange(col_tiles)[:, None]) & valid[None, :]
    return jnp.einsum(
        "ts,src->trc", owner.astype(jnp.float32), products, precision=lax.Precision.HIGHEST
    )


def on_device(lam, integrals, occ_sym, cd_sym, ab_sym):
    row_tiles = occ_sym.shape[0]
    cd_tiles = cd_sym.shape[0]
    tile_edge = lam.shape[0] // row_tiles
    col_tiles = ab_sym.shape[0]
    own_cols = integrals.shape[1] // tile_edge
    peers = col_tiles // own_cols
    row_of = jnp.argmax(occ_sym[None, :] == ab_sym[:, None], axis=1)
    kept = cd_sym[:, None] == ab_sym[None, :]
    kept = kept.reshape(cd_tiles, peers, own_cols).transpose(1, 0, 2)
    need = doubling_max(jnp.max(jnp.sum(kept, axis=(1, 2))), "vir")
    dense = cd_tiles * own_cols
    caps = sorted({max(1, dense // 4), max(1, dense // 3), max(1, dense // 2), dense})
    branch = sum((need > cap).astype(jnp.int32) for cap in caps[:-1])
    partial_sum = lax.switch(
        branch,
        [
            lambda l, i, cap=cap: packed_partials(l, i, kept, row_of, cap, tile_edge)
            for cap in caps
        ],
        lam,
        integrals,
    )
    summed = halving_reduce_scatter(partial_sum, "vir")
    own_row = row_of[lax.axis_index("vir")]
    keep = (jnp.arange(row_tiles) == own_row)[:, None, None]
    out = jnp.where(keep, summed.astype(jnp.bfloat16)[None], jnp.zeros((), jnp.bfloat16))
    return out.reshape(row_tiles * tile_edge, summed.shape[1])


def solution(mesh):
    in_specs = (P("occ", "vir"), P("vir", "occ"), P("occ"), P("vir"), P())
    out_specs = P("occ", "vir")
    return jax.shard_map(
        on_device, mesh=mesh, in_specs=in_specs, out_specs=out_specs, check_vma=False
    )
```

```python
import jax
import jax.numpy as jnp
from jax import lax
from jax.sharding import PartitionSpec as P


def halving_reduce_scatter(parts, axis):
    n = lax.axis_size(axis)
    me = lax.axis_index(axis)
    step = 1
    while step < n:
        bit = (me // step) % 2
        pairs = parts.reshape(parts.shape[0] // 2, 2, *parts.shape[1:])
        keep = lax.dynamic_index_in_dim(pairs, bit, axis=1, keepdims=False)
        send = lax.dynamic_index_in_dim(pairs, 1 - bit, axis=1, keepdims=False)
        perm = [(j, j ^ step) for j in range(n)]
        parts = keep + lax.ppermute(send, axis, perm)
        step *= 2
    return parts[0]


def doubling_max(value, axis):
    n = lax.axis_size(axis)
    step = 1
    while step < n:
        value = jnp.maximum(value, lax.ppermute(value, axis, [(j, j ^ step) for j in range(n)]))
        step *= 2
    return value


def packed_partials(lam, integrals, kept, row_of, cap, edge):
    peers, cd_tiles, own_cols = kept.shape
    col_tiles = peers * own_cols
    flat = kept.reshape(peers, cd_tiles * own_cols)
    rank = jnp.cumsum(flat, axis=1) - 1
    hit = flat[:, None, :] & (rank[:, None, :] == jnp.arange(cap)[None, :, None])
    order = jnp.sum(hit * jnp.arange(cd_tiles * own_cols), axis=2)
    valid = jnp.any(hit, axis=2)
    q = order // own_cols
    c = order % own_cols
    me = lax.axis_index("occ")
    blocks = integrals.reshape(cd_tiles, edge, own_cols, edge)[q[me]]
    sent = blocks[:, :, 0]
    for col in range(1, own_cols):
        sent = jnp.where((c[me] == col)[:, None, None], blocks[:, :, col], sent)
    received = lax.all_gather(sent, "occ", axis=0, tiled=True)
    t = (jnp.arange(peers)[:, None] * own_cols + c).reshape(-1)
    valid = valid.reshape(-1)
    row_tiles = lam.shape[0] // edge
    lam_grid = lam.reshape(row_tiles, edge, cd_tiles, edge).transpose(0, 2, 1, 3)
    lam_grid = lam_grid.reshape(row_tiles * cd_tiles, edge, edge)
    lam_tiles = lam_grid[row_of[t] * cd_tiles + q.reshape(-1)]
    lam_tiles = jnp.where(valid[:, None, None], lam_tiles, jnp.zeros((), lam.dtype))
    products = jnp.einsum(
        "srm,smc->src", lam_tiles, received, preferred_element_type=jnp.float32
    )
    owner = (t[None, :] == jnp.arange(col_tiles)[:, None]) & valid[None, :]
    return jnp.einsum(
        "ts,src->trc", owner.astype(jnp.float32), products, precision=lax.Precision.HIGHEST
    )


def on_device(lam, integrals, occ_sym, cd_sym, ab_sym):
    row_tiles = occ_sym.shape[0]
    cd_tiles = cd_sym.shape[0]
    tile_edge = lam.shape[0] // row_tiles
    col_tiles = ab_sym.shape[0]
    own_cols = integrals.shape[1] // tile_edge
    peers = col_tiles // own_cols
    row_of = jnp.argmax(occ_sym[None, :] == ab_sym[:, None], axis=1)
    kept = cd_sym[:, None] == ab_sym[None, :]
    kept = kept.reshape(cd_tiles, peers, own_cols).transpose(1, 0, 2)
    need = doubling_max(jnp.max(jnp.sum(kept, axis=(1, 2))), "vir")
    dense = cd_tiles * own_cols
    caps = sorted({max(1, dense // 3), max(1, dense // 2), dense})
    branch = sum((need > cap).astype(jnp.int32) for cap in caps[:-1])
    partial_sum = lax.switch(
        branch,
        [
            lambda l, i, cap=cap: packed_partials(l, i, kept, row_of, cap, tile_edge)
            for cap in caps
        ],
        lam,
        integrals,
    )
    summed = halving_reduce_scatter(partial_sum, "vir")
    own_row = row_of[lax.axis_index("vir")]
    keep = (jnp.arange(row_tiles) == own_row)[:, None, None]
    out = jnp.where(keep, summed.astype(jnp.bfloat16)[None], jnp.zeros((), jnp.bfloat16))
    return out.reshape(row_tiles * tile_edge, summed.shape[1])


def solution(mesh):
    in_specs = (P("occ", "vir"), P("vir", "occ"), P("occ"), P("vir"), P())
    out_specs = P("occ", "vir")
    return jax.shard_map(
        on_device, mesh=mesh, in_specs=in_specs, out_specs=out_specs, check_vma=False
    )
```

```python
import jax
import jax.numpy as jnp
from jax import lax
from jax.sharding import PartitionSpec as P


def halving_reduce_scatter(parts, axis):
    n = lax.axis_size(axis)
    me = lax.axis_index(axis)
    step = 1
    while step < n:
        bit = (me // step) % 2
        pairs = parts.reshape(parts.shape[0] // 2, 2, *parts.shape[1:])
        keep = lax.dynamic_index_in_dim(pairs, bit, axis=1, keepdims=False)
        send = lax.dynamic_index_in_dim(pairs, 1 - bit, axis=1, keepdims=False)
        perm = [(j, j ^ step) for j in range(n)]
        parts = keep + lax.ppermute(send, axis, perm)
        step *= 2
    return parts[0]


def doubling_max(value, axis):
    n = lax.axis_size(axis)
    step = 1
    while step < n:
        value = jnp.maximum(value, lax.ppermute(value, axis, [(j, j ^ step) for j in range(n)]))
        step *= 2
    return value


def packed_partials(lam_kept, int_kept, order, valid, col_of, col_tiles, cap):
    peers = order.shape[0]
    received = lax.all_gather(int_kept[:cap], "occ", axis=0, tiled=True)
    q = order[:, :cap].reshape(-1)
    t = col_of.reshape(peers, -1)[:, :cap].reshape(-1)
    ok = valid[:, :cap].reshape(-1)
    lam_tiles = jnp.where(ok[:, None, None], lam_kept[q], jnp.zeros((), lam_kept.dtype))
    products = jnp.einsum(
        "srm,smc->src", lam_tiles, received, preferred_element_type=jnp.float32
    )
    owner = (t[None, :] == jnp.arange(col_tiles)[:, None]) & ok[None, :]
    return jnp.einsum(
        "ts,src->trc", owner.astype(jnp.float32), products, precision=lax.Precision.HIGHEST
    )


def on_device(lam, integrals, occ_sym, cd_sym, ab_sym):
    row_tiles = occ_sym.shape[0]
    cd_tiles = cd_sym.shape[0]
    tile_edge = lam.shape[0] // row_tiles
    col_tiles = ab_sym.shape[0]
    own_cols = integrals.shape[1] // tile_edge
    peers = col_tiles // own_cols
    row_of = jnp.argmax(occ_sym[None, :] == ab_sym[:, None], axis=1)
    kept = cd_sym[:, None] == ab_sym[None, :]
    kept = kept.reshape(cd_tiles, peers, own_cols).transpose(1, 0, 2)
    need = doubling_max(jnp.max(jnp.sum(kept, axis=(1, 2))), "vir")
    dense = cd_tiles * own_cols
    flat = kept.reshape(peers, dense)
    rank = jnp.cumsum(flat, axis=1) - 1
    hit = flat[:, None, :] & (rank[:, None, :] == jnp.arange(dense)[None, :, None])
    slot = jnp.sum(hit * jnp.arange(dense), axis=2)
    valid = jnp.any(hit, axis=2)
    order = slot // own_cols
    col_of = jnp.arange(peers)[:, None] * own_cols + slot % own_cols
    me = lax.axis_index("occ")
    blocks = integrals.reshape(cd_tiles, tile_edge, own_cols * tile_edge)[order[me]]
    int_kept = blocks[:, :, :tile_edge]
    for col in range(1, own_cols):
        pick = (slot[me] % own_cols == col)[:, None, None]
        int_kept = jnp.where(pick, blocks[:, :, col * tile_edge:(col + 1) * tile_edge], int_kept)
    row_for_q = jnp.argmax(occ_sym[:, None] == cd_sym[None, :], axis=0)
    lam4 = lam.reshape(row_tiles, tile_edge, cd_tiles, tile_edge)
    pick = (row_for_q[None, :] == jnp.arange(row_tiles)[:, None])[:, None, :, None]
    lam_kept = jnp.sum(jnp.where(pick, lam4, jnp.zeros((), lam.dtype)), axis=0)
    lam_kept = lam_kept.transpose(1, 0, 2)
    caps = sorted({max(1, dense // 3), max(1, dense // 2), dense})
    branch = sum((need > cap).astype(jnp.int32) for cap in caps[:-1])
    partial_sum = lax.switch(
        branch,
        [
            lambda l, i, cap=cap: packed_partials(l, i, order, valid, col_of, col_tiles, cap)
            for cap in caps
        ],
        lam_kept,
        int_kept,
    )
    summed = halving_reduce_scatter(partial_sum, "vir")
    own_row = row_of[lax.axis_index("vir")]
    keep = (jnp.arange(row_tiles) == own_row)[:, None, None]
    out = jnp.where(keep, summed.astype(jnp.bfloat16)[None], jnp.zeros((), jnp.bfloat16))
    return out.reshape(row_tiles * tile_edge, summed.shape[1])


def solution(mesh):
    in_specs = (P("occ", "vir"), P("vir", "occ"), P("occ"), P("vir"), P())
    out_specs = P("occ", "vir")
    return jax.shard_map(
        on_device, mesh=mesh, in_specs=in_specs, out_specs=out_specs, check_vma=False
    )
```

```python
import jax
import jax.numpy as jnp
from jax import lax
from jax.sharding import PartitionSpec as P


def halving_reduce_scatter(parts, axis):
    n = lax.axis_size(axis)
    me = lax.axis_index(axis)
    step = 1
    while step < n:
        bit = (me // step) % 2
        pairs = parts.reshape(parts.shape[0] // 2, 2, *parts.shape[1:])
        keep = lax.dynamic_index_in_dim(pairs, bit, axis=1, keepdims=False)
        send = lax.dynamic_index_in_dim(pairs, 1 - bit, axis=1, keepdims=False)
        perm = [(j, j ^ step) for j in range(n)]
        parts = keep + lax.ppermute(send, axis, perm)
        step *= 2
    return parts[0]


def doubling_max(value, axis):
    n = lax.axis_size(axis)
    step = 1
    while step < n:
        value = jnp.maximum(value, lax.ppermute(value, axis, [(j, j ^ step) for j in range(n)]))
        step *= 2
    return value


def packed_partials(lam_kept, int_kept, order, valid, col_of, col_tiles, cap):
    peers = order.shape[0]
    received = lax.all_gather(int_kept[:cap], "occ", axis=0, tiled=True)
    q = order[:, :cap].reshape(-1)
    t = col_of.reshape(peers, -1)[:, :cap].reshape(-1)
    ok = valid[:, :cap].reshape(-1)
    lam_tiles = jnp.where(ok[:, None, None], lam_kept[q], jnp.zeros((), lam_kept.dtype))
    products = jnp.einsum(
        "srm,smc->src", lam_tiles, received, preferred_element_type=jnp.float32
    )
    owner = (t[None, :] == jnp.arange(col_tiles)[:, None]) & ok[None, :]
    return jnp.einsum(
        "ts,src->trc", owner.astype(jnp.float32), products, precision=lax.Precision.HIGHEST
    )


def on_device(lam, integrals, occ_sym, cd_sym, ab_sym):
    row_tiles = occ_sym.shape[0]
    cd_tiles = cd_sym.shape[0]
    tile_edge = lam.shape[0] // row_tiles
    col_tiles = ab_sym.shape[0]
    own_cols = integrals.shape[1] // tile_edge
    peers = col_tiles // own_cols
    row_of = jnp.argmax(occ_sym[None, :] == ab_sym[:, None], axis=1)
    kept = cd_sym[:, None] == ab_sym[None, :]
    kept = kept.reshape(cd_tiles, peers, own_cols).transpose(1, 0, 2)
    need = doubling_max(jnp.max(jnp.sum(kept, axis=(1, 2))), "vir")
    dense = cd_tiles * own_cols
    flat = kept.reshape(peers, dense)
    rank = jnp.cumsum(flat, axis=1) - 1
    hit = flat[:, None, :] & (rank[:, None, :] == jnp.arange(dense)[None, :, None])
    slot = jnp.sum(hit * jnp.arange(dense), axis=2)
    valid = jnp.any(hit, axis=2)
    order = slot // own_cols
    col_of = jnp.arange(peers)[:, None] * own_cols + slot % own_cols
    me = lax.axis_index("occ")
    blocks = integrals.reshape(cd_tiles, tile_edge, own_cols * tile_edge)[order[me]]
    int_kept = blocks[:, :, :tile_edge]
    for col in range(1, own_cols):
        pick = (slot[me] % own_cols == col)[:, None, None]
        int_kept = jnp.where(pick, blocks[:, :, col * tile_edge:(col + 1) * tile_edge], int_kept)
    row_for_q = jnp.argmax(occ_sym[:, None] == cd_sym[None, :], axis=0)
    lam3 = lam.reshape(row_tiles, tile_edge, cd_tiles * tile_edge)
    pick = jnp.repeat(row_for_q[None, :] == jnp.arange(row_tiles)[:, None], tile_edge, axis=1)
    lam_kept = jnp.sum(jnp.where(pick[:, None, :], lam3, jnp.zeros((), lam.dtype)), axis=0)
    lam_kept = lam_kept.reshape(tile_edge, cd_tiles, tile_edge).transpose(1, 0, 2)
    caps = sorted({max(1, dense // 3), max(1, dense // 2), dense})
    branch = sum((need > cap).astype(jnp.int32) for cap in caps[:-1])
    partial_sum = lax.switch(
        branch,
        [
            lambda l, i, cap=cap: packed_partials(l, i, order, valid, col_of, col_tiles, cap)
            for cap in caps
        ],
        lam_kept,
        int_kept,
    )
    summed = halving_reduce_scatter(partial_sum, "vir")
    own_row = row_of[lax.axis_index("vir")]
    keep = (jnp.arange(row_tiles) == own_row)[:, None, None]
    out = jnp.where(keep, summed.astype(jnp.bfloat16)[None], jnp.zeros((), jnp.bfloat16))
    return out.reshape(row_tiles * tile_edge, summed.shape[1])


def solution(mesh):
    in_specs = (P("occ", "vir"), P("vir", "occ"), P("occ"), P("vir"), P())
    out_specs = P("occ", "vir")
    return jax.shard_map(
        on_device, mesh=mesh, in_specs=in_specs, out_specs=out_specs, check_vma=False
    )
```

```python
import jax
import jax.numpy as jnp
from jax import lax
from jax.sharding import PartitionSpec as P


def halving_reduce_scatter(parts, axis):
    n = lax.axis_size(axis)
    me = lax.axis_index(axis)
    step = 1
    while step < n:
        bit = (me // step) % 2
        pairs = parts.reshape(parts.shape[0] // 2, 2, *parts.shape[1:])
        keep = lax.dynamic_index_in_dim(pairs, bit, axis=1, keepdims=False)
        send = lax.dynamic_index_in_dim(pairs, 1 - bit, axis=1, keepdims=False)
        perm = [(j, j ^ step) for j in range(n)]
        parts = keep + lax.ppermute(send, axis, perm)
        step *= 2
    return parts[0]


def doubling_max(value, axis):
    n = lax.axis_size(axis)
    step = 1
    while step < n:
        value = jnp.maximum(value, lax.ppermute(value, axis, [(j, j ^ step) for j in range(n)]))
        step *= 2
    return value


def packed_partials(lam_kept, int_kept, order, valid, col_of, col_tiles, cap):
    peers = order.shape[0]
    received = lax.all_gather(int_kept[:cap], "occ", axis=0, tiled=True)
    q = order[:, :cap].reshape(-1)
    t = col_of.reshape(peers, -1)[:, :cap].reshape(-1)
    ok = valid[:, :cap].reshape(-1)
    lam_tiles = jnp.where(ok[:, None, None], lam_kept[q], jnp.zeros((), lam_kept.dtype))
    products = jnp.einsum(
        "srm,smc->src", lam_tiles, received, preferred_element_type=jnp.float32
    )
    owner = (t[None, :] == jnp.arange(col_tiles)[:, None]) & ok[None, :]
    return jnp.einsum(
        "ts,src->trc", owner.astype(jnp.float32), products, precision=lax.Precision.HIGHEST
    )


def on_device(lam, integrals, occ_sym, cd_sym, ab_sym):
    row_tiles = occ_sym.shape[0]
    cd_tiles = cd_sym.shape[0]
    tile_edge = lam.shape[0] // row_tiles
    col_tiles = ab_sym.shape[0]
    own_cols = integrals.shape[1] // tile_edge
    peers = col_tiles // own_cols
    row_of = jnp.argmax(occ_sym[None, :] == ab_sym[:, None], axis=1)
    kept = cd_sym[:, None] == ab_sym[None, :]
    kept = kept.reshape(cd_tiles, peers, own_cols).transpose(1, 0, 2)
    need = lax.pmax(jnp.max(jnp.sum(kept, axis=(1, 2))), "vir")
    dense = cd_tiles * own_cols
    flat = kept.reshape(peers, dense)
    rank = jnp.cumsum(flat, axis=1) - 1
    hit = flat[:, None, :] & (rank[:, None, :] == jnp.arange(dense)[None, :, None])
    slot = jnp.sum(hit * jnp.arange(dense), axis=2)
    valid = jnp.any(hit, axis=2)
    order = slot // own_cols
    col_of = jnp.arange(peers)[:, None] * own_cols + slot % own_cols
    me = lax.axis_index("occ")
    blocks = integrals.reshape(cd_tiles, tile_edge, own_cols * tile_edge)[order[me]]
    int_kept = blocks[:, :, :tile_edge]
    for col in range(1, own_cols):
        pick = (slot[me] % own_cols == col)[:, None, None]
        int_kept = jnp.where(pick, blocks[:, :, col * tile_edge:(col + 1) * tile_edge], int_kept)
    row_for_q = jnp.argmax(occ_sym[:, None] == cd_sym[None, :], axis=0)
    lam3 = lam.reshape(row_tiles, tile_edge, cd_tiles * tile_edge)
    pick = jnp.repeat(row_for_q[None, :] == jnp.arange(row_tiles)[:, None], tile_edge, axis=1)
    lam_kept = jnp.sum(jnp.where(pick[:, None, :], lam3, jnp.zeros((), lam.dtype)), axis=0)
    lam_kept = lam_kept.reshape(tile_edge, cd_tiles, tile_edge).transpose(1, 0, 2)
    caps = sorted({max(1, dense // 3), max(1, dense // 2), dense})
    branch = sum((need > cap).astype(jnp.int32) for cap in caps[:-1])
    partial_sum = lax.switch(
        branch,
        [
            lambda l, i, cap=cap: packed_partials(l, i, order, valid, col_of, col_tiles, cap)
            for cap in caps
        ],
        lam_kept,
        int_kept,
    )
    summed = halving_reduce_scatter(partial_sum, "vir")
    own_row = row_of[lax.axis_index("vir")]
    keep = (jnp.arange(row_tiles) == own_row)[:, None, None]
    out = jnp.where(keep, summed.astype(jnp.bfloat16)[None], jnp.zeros((), jnp.bfloat16))
    return out.reshape(row_tiles * tile_edge, summed.shape[1])


def solution(mesh):
    in_specs = (P("occ", "vir"), P("vir", "occ"), P("occ"), P("vir"), P())
    out_specs = P("occ", "vir")
    return jax.shard_map(
        on_device, mesh=mesh, in_specs=in_specs, out_specs=out_specs, check_vma=False
    )
```

```python
import jax
import jax.numpy as jnp
from jax import lax
from jax.sharding import PartitionSpec as P


def halving_reduce_scatter(parts, axis):
    n = lax.axis_size(axis)
    me = lax.axis_index(axis)
    step = 1
    while step < n:
        bit = (me // step) % 2
        pairs = parts.reshape(parts.shape[0] // 2, 2, *parts.shape[1:])
        keep = lax.dynamic_index_in_dim(pairs, bit, axis=1, keepdims=False)
        send = lax.dynamic_index_in_dim(pairs, 1 - bit, axis=1, keepdims=False)
        perm = [(j, j ^ step) for j in range(n)]
        parts = keep + lax.ppermute(send, axis, perm)
        step *= 2
    return parts[0]


def doubling_max(value, axis):
    n = lax.axis_size(axis)
    step = 1
    while step < n:
        value = jnp.maximum(value, lax.ppermute(value, axis, [(j, j ^ step) for j in range(n)]))
        step *= 2
    return value


def line_gather(x, axis):
    n = lax.axis_size(axis)
    me = lax.axis_index(axis)
    rightward = [(a, a + 1) for a in range(n - 1)]
    leftward = [(a, a - 1) for a in range(1, n)]
    lefts, rights = [], []
    from_left, from_right = x, x
    for _ in range(1, n):
        from_left = lax.ppermute(from_left, axis, rightward)
        from_right = lax.ppermute(from_right, axis, leftward)
        lefts.append(from_left)
        rights.append(from_right)
    line = jnp.concatenate(lefts[::-1] + [x] + rights)
    return lax.dynamic_slice_in_dim(line, (n - 1 - me) * x.shape[0], n * x.shape[0])


def packed_partials(lam_kept, int_kept, order, valid, col_of, col_tiles, cap):
    received = line_gather(int_kept[:cap], "occ")
    q = order[:, :cap].reshape(-1)
    t = col_of[:, :cap].reshape(-1)
    ok = valid[:, :cap].reshape(-1)
    lam_tiles = jnp.where(ok[:, None, None], lam_kept[q], jnp.zeros((), lam_kept.dtype))
    products = jnp.einsum(
        "srm,smc->src", lam_tiles, received, preferred_element_type=jnp.float32
    )
    onehot = (t[None, :] == jnp.arange(col_tiles)[:, None]) & ok[None, :]
    return jnp.einsum(
        "ts,src->trc", onehot.astype(jnp.float32), products, precision=lax.Precision.HIGHEST
    )


def on_device(lam, integrals, occ_sym, cd_sym, ab_sym):
    row_tiles = occ_sym.shape[0]
    cd_tiles = cd_sym.shape[0]
    tile_edge = lam.shape[0] // row_tiles
    col_tiles = ab_sym.shape[0]
    own_cols = integrals.shape[1] // tile_edge
    peers = col_tiles // own_cols
    row_of = jnp.argmax(occ_sym[None, :] == ab_sym[:, None], axis=1)
    kept = cd_sym[:, None] == ab_sym[None, :]
    kept = kept.reshape(cd_tiles, peers, own_cols).transpose(1, 0, 2)
    need = lax.pmax(jnp.max(jnp.sum(kept, axis=(1, 2))), "vir")
    dense = cd_tiles * own_cols
    flat = kept.reshape(peers, dense)
    rank = jnp.cumsum(flat, axis=1) - 1
    hit = flat[:, None, :] & (rank[:, None, :] == jnp.arange(dense)[None, :, None])
    slot = jnp.sum(hit * jnp.arange(dense), axis=2)
    valid = jnp.any(hit, axis=2)
    order = slot // own_cols
    col_of = jnp.arange(peers)[:, None] * own_cols + slot % own_cols
    me = lax.axis_index("occ")
    blocks = integrals.reshape(cd_tiles, tile_edge, own_cols * tile_edge)[order[me]]
    int_kept = blocks[:, :, :tile_edge]
    for col in range(1, own_cols):
        pick = (slot[me] % own_cols == col)[:, None, None]
        int_kept = jnp.where(pick, blocks[:, :, col * tile_edge:(col + 1) * tile_edge], int_kept)
    row_for_q = jnp.argmax(occ_sym[:, None] == cd_sym[None, :], axis=0)
    lam3 = lam.reshape(row_tiles, tile_edge, cd_tiles * tile_edge)
    pick = jnp.repeat(row_for_q[None, :] == jnp.arange(row_tiles)[:, None], tile_edge, axis=1)
    lam_kept = jnp.sum(jnp.where(pick[:, None, :], lam3, jnp.zeros((), lam.dtype)), axis=0)
    lam_kept = lam_kept.reshape(tile_edge, cd_tiles, tile_edge).transpose(1, 0, 2)
    caps = sorted({max(1, dense // 3), max(1, dense // 2), dense})
    branch = sum((need > cap).astype(jnp.int32) for cap in caps[:-1])
    partial_sum = lax.switch(
        branch,
        [
            lambda l, i, cap=cap: packed_partials(l, i, order, valid, col_of, col_tiles, cap)
            for cap in caps
        ],
        lam_kept,
        int_kept,
    )
    summed = halving_reduce_scatter(partial_sum, "vir")
    own_row = row_of[lax.axis_index("vir")]
    keep = (jnp.arange(row_tiles) == own_row)[:, None, None]
    out = jnp.where(keep, summed.astype(jnp.bfloat16)[None], jnp.zeros((), jnp.bfloat16))
    return out.reshape(row_tiles * tile_edge, summed.shape[1])


def solution(mesh):
    in_specs = (P("occ", "vir"), P("vir", "occ"), P("occ"), P("vir"), P())
    out_specs = P("occ", "vir")
    return jax.shard_map(
        on_device, mesh=mesh, in_specs=in_specs, out_specs=out_specs, check_vma=False
    )
```

```python
import jax
import jax.numpy as jnp
from jax import lax
from jax.sharding import PartitionSpec as P


def halving_reduce_scatter(parts, axis):
    n = lax.axis_size(axis)
    me = lax.axis_index(axis)
    step = 1
    while step < n:
        bit = (me // step) % 2
        pairs = parts.reshape(parts.shape[0] // 2, 2, *parts.shape[1:])
        keep = lax.dynamic_index_in_dim(pairs, bit, axis=1, keepdims=False)
        send = lax.dynamic_index_in_dim(pairs, 1 - bit, axis=1, keepdims=False)
        perm = [(j, j ^ step) for j in range(n)]
        parts = keep + lax.ppermute(send, axis, perm)
        step *= 2
    return parts[0]


def doubling_max(value, axis):
    n = lax.axis_size(axis)
    step = 1
    while step < n:
        value = jnp.maximum(value, lax.ppermute(value, axis, [(j, j ^ step) for j in range(n)]))
        step *= 2
    return value


def line_gather(x, axis):
    n = lax.axis_size(axis)
    me = lax.axis_index(axis)
    rightward = [(a, a + 1) for a in range(n - 1)]
    leftward = [(a, a - 1) for a in range(1, n)]
    lefts, rights = [], []
    from_left, from_right = x, x
    for _ in range(1, n):
        from_left = lax.ppermute(from_left, axis, rightward)
        from_right = lax.ppermute(from_right, axis, leftward)
        lefts.append(from_left)
        rights.append(from_right)
    line = jnp.concatenate(lefts[::-1] + [x] + rights)
    return lax.dynamic_slice_in_dim(line, (n - 1 - me) * x.shape[0], n * x.shape[0])


def packed_partials(lam_kept, int_kept, order, valid, col_of, col_tiles, cap):
    received = line_gather(int_kept[:cap], "occ")
    q = order[:, :cap].reshape(-1)
    t = col_of[:, :cap].reshape(-1)
    ok = valid[:, :cap].reshape(-1)
    lam_tiles = jnp.where(ok[:, None, None], lam_kept[q], jnp.zeros((), lam_kept.dtype))
    products = jnp.einsum(
        "srm,smc->src", lam_tiles, received, preferred_element_type=jnp.float32
    )
    onehot = (t[None, :] == jnp.arange(col_tiles)[:, None]) & ok[None, :]
    return jnp.einsum(
        "ts,src->trc", onehot.astype(jnp.float32), products, precision=lax.Precision.HIGHEST
    )


def on_device(lam, integrals, occ_sym, cd_sym, ab_sym):
    row_tiles = occ_sym.shape[0]
    cd_tiles = cd_sym.shape[0]
    tile_edge = lam.shape[0] // row_tiles
    col_tiles = ab_sym.shape[0]
    own_cols = integrals.shape[1] // tile_edge
    peers = col_tiles // own_cols
    row_of = jnp.argmax(occ_sym[None, :] == ab_sym[:, None], axis=1)
    kept = cd_sym[:, None] == ab_sym[None, :]
    kept = kept.reshape(cd_tiles, peers, own_cols).transpose(1, 0, 2)
    need = jnp.max(jnp.sum(kept, axis=(1, 2)))
    dense = cd_tiles * own_cols
    flat = kept.reshape(peers, dense)
    rank = jnp.cumsum(flat, axis=1) - 1
    hit = flat[:, None, :] & (rank[:, None, :] == jnp.arange(dense)[None, :, None])
    slot = jnp.sum(hit * jnp.arange(dense), axis=2)
    valid = jnp.any(hit, axis=2)
    order = slot // own_cols
    col_of = jnp.arange(peers)[:, None] * own_cols + slot % own_cols
    me = lax.axis_index("occ")
    blocks = integrals.reshape(cd_tiles, tile_edge, own_cols * tile_edge)[order[me]]
    int_kept = blocks[:, :, :tile_edge]
    for col in range(1, own_cols):
        pick = (slot[me] % own_cols == col)[:, None, None]
        int_kept = jnp.where(pick, blocks[:, :, col * tile_edge:(col + 1) * tile_edge], int_kept)
    row_for_q = jnp.argmax(occ_sym[:, None] == cd_sym[None, :], axis=0)
    lam3 = lam.reshape(row_tiles, tile_edge, cd_tiles * tile_edge)
    pick = jnp.repeat(row_for_q[None, :] == jnp.arange(row_tiles)[:, None], tile_edge, axis=1)
    lam_kept = jnp.sum(jnp.where(pick[:, None, :], lam3, jnp.zeros((), lam.dtype)), axis=0)
    lam_kept = lam_kept.reshape(tile_edge, cd_tiles, tile_edge).transpose(1, 0, 2)
    caps = sorted({max(1, dense // 3), max(1, dense // 2), dense})
    branch = sum((need > cap).astype(jnp.int32) for cap in caps[:-1])
    partial_sum = lax.switch(
        branch,
        [
            lambda l, i, cap=cap: packed_partials(l, i, order, valid, col_of, col_tiles, cap)
            for cap in caps
        ],
        lam_kept,
        int_kept,
    )
    summed = halving_reduce_scatter(partial_sum, "vir")
    own_row = row_of[lax.axis_index("vir")]
    keep = (jnp.arange(row_tiles) == own_row)[:, None, None]
    out = jnp.where(keep, summed.astype(jnp.bfloat16)[None], jnp.zeros((), jnp.bfloat16))
    return out.reshape(row_tiles * tile_edge, summed.shape[1])


def solution(mesh):
    in_specs = (P("occ", "vir"), P("vir", "occ"), P("occ"), P("vir"), P())
    out_specs = P("occ", "vir")
    return jax.shard_map(
        on_device, mesh=mesh, in_specs=in_specs, out_specs=out_specs, check_vma=False
    )
```

```python
import jax
import jax.numpy as jnp
from jax import lax
from jax.sharding import PartitionSpec as P


def halving_reduce_scatter(parts, axis):
    n = lax.axis_size(axis)
    me = lax.axis_index(axis)
    step = 1
    while step < n:
        bit = (me // step) % 2
        pairs = parts.reshape(parts.shape[0] // 2, 2, *parts.shape[1:])
        keep = lax.dynamic_index_in_dim(pairs, bit, axis=1, keepdims=False)
        send = lax.dynamic_index_in_dim(pairs, 1 - bit, axis=1, keepdims=False)
        perm = [(j, j ^ step) for j in range(n)]
        parts = keep + lax.ppermute(send, axis, perm)
        step *= 2
    return parts[0]


def doubling_max(value, axis):
    n = lax.axis_size(axis)
    step = 1
    while step < n:
        value = jnp.maximum(value, lax.ppermute(value, axis, [(j, j ^ step) for j in range(n)]))
        step *= 2
    return value


def line_gather(x, axis):
    n = lax.axis_size(axis)
    me = lax.axis_index(axis)
    lefts, rights = [], []
    for dist in range(1, n):
        lefts.append(lax.ppermute(x, axis, [(a, a + dist) for a in range(n - dist)]))
        rights.append(lax.ppermute(x, axis, [(a, a - dist) for a in range(dist, n)]))
    line = jnp.concatenate(lefts[::-1] + [x] + rights)
    return lax.dynamic_slice_in_dim(line, (n - 1 - me) * x.shape[0], n * x.shape[0])


def packed_partials(lam_kept, int_kept, order, valid, col_of, col_tiles, cap):
    received = line_gather(int_kept[:cap], "occ")
    q = order[:, :cap].reshape(-1)
    t = col_of[:, :cap].reshape(-1)
    ok = valid[:, :cap].reshape(-1)
    lam_tiles = jnp.where(ok[:, None, None], lam_kept[q], jnp.zeros((), lam_kept.dtype))
    products = jnp.einsum(
        "srm,smc->src", lam_tiles, received, preferred_element_type=jnp.float32
    )
    onehot = (t[None, :] == jnp.arange(col_tiles)[:, None]) & ok[None, :]
    return jnp.einsum(
        "ts,src->trc", onehot.astype(jnp.float32), products, precision=lax.Precision.HIGHEST
    )


def on_device(lam, integrals, occ_sym, cd_sym, ab_sym):
    row_tiles = occ_sym.shape[0]
    cd_tiles = cd_sym.shape[0]
    tile_edge = lam.shape[0] // row_tiles
    col_tiles = ab_sym.shape[0]
    own_cols = integrals.shape[1] // tile_edge
    peers = col_tiles // own_cols
    row_of = jnp.argmax(occ_sym[None, :] == ab_sym[:, None], axis=1)
    kept = cd_sym[:, None] == ab_sym[None, :]
    kept = kept.reshape(cd_tiles, peers, own_cols).transpose(1, 0, 2)
    need = jnp.max(jnp.sum(kept, axis=(1, 2)))
    dense = cd_tiles * own_cols
    flat = kept.reshape(peers, dense)
    rank = jnp.cumsum(flat, axis=1) - 1
    hit = flat[:, None, :] & (rank[:, None, :] == jnp.arange(dense)[None, :, None])
    slot = jnp.sum(hit * jnp.arange(dense), axis=2)
    valid = jnp.any(hit, axis=2)
    order = slot // own_cols
    col_of = jnp.arange(peers)[:, None] * own_cols + slot % own_cols
    me = lax.axis_index("occ")
    blocks = integrals.reshape(cd_tiles, tile_edge, own_cols * tile_edge)[order[me]]
    int_kept = blocks[:, :, :tile_edge]
    for col in range(1, own_cols):
        pick = (slot[me] % own_cols == col)[:, None, None]
        int_kept = jnp.where(pick, blocks[:, :, col * tile_edge:(col + 1) * tile_edge], int_kept)
    row_for_q = jnp.argmax(occ_sym[:, None] == cd_sym[None, :], axis=0)
    lam3 = lam.reshape(row_tiles, tile_edge, cd_tiles * tile_edge)
    pick = jnp.repeat(row_for_q[None, :] == jnp.arange(row_tiles)[:, None], tile_edge, axis=1)
    lam_kept = jnp.sum(jnp.where(pick[:, None, :], lam3, jnp.zeros((), lam.dtype)), axis=0)
    lam_kept = lam_kept.reshape(tile_edge, cd_tiles, tile_edge).transpose(1, 0, 2)
    caps = sorted({max(1, dense // 3), max(1, dense // 2), dense})
    branch = sum((need > cap).astype(jnp.int32) for cap in caps[:-1])
    partial_sum = lax.switch(
        branch,
        [
            lambda l, i, cap=cap: packed_partials(l, i, order, valid, col_of, col_tiles, cap)
            for cap in caps
        ],
        lam_kept,
        int_kept,
    )
    summed = halving_reduce_scatter(partial_sum, "vir")
    own_row = row_of[lax.axis_index("vir")]
    keep = (jnp.arange(row_tiles) == own_row)[:, None, None]
    out = jnp.where(keep, summed.astype(jnp.bfloat16)[None], jnp.zeros((), jnp.bfloat16))
    return out.reshape(row_tiles * tile_edge, summed.shape[1])


def solution(mesh):
    in_specs = (P("occ", "vir"), P("vir", "occ"), P("occ"), P("vir"), P())
    out_specs = P("occ", "vir")
    return jax.shard_map(
        on_device, mesh=mesh, in_specs=in_specs, out_specs=out_specs, check_vma=False
    )
```

```python
import jax
import jax.numpy as jnp
from jax import lax
from jax.sharding import PartitionSpec as P


def halving_reduce_scatter(parts, axis):
    n = lax.axis_size(axis)
    me = lax.axis_index(axis)
    step = 1
    while step < n:
        bit = (me // step) % 2
        pairs = parts.reshape(parts.shape[0] // 2, 2, *parts.shape[1:])
        keep = lax.dynamic_index_in_dim(pairs, bit, axis=1, keepdims=False)
        send = lax.dynamic_index_in_dim(pairs, 1 - bit, axis=1, keepdims=False)
        perm = [(j, j ^ step) for j in range(n)]
        parts = keep + lax.ppermute(send, axis, perm)
        step *= 2
    return parts[0]


def doubling_max(value, axis):
    n = lax.axis_size(axis)
    step = 1
    while step < n:
        value = jnp.maximum(value, lax.ppermute(value, axis, [(j, j ^ step) for j in range(n)]))
        step *= 2
    return value


def line_gather(x, axis):
    n = lax.axis_size(axis)
    me = lax.axis_index(axis)
    rightward = [(a, a + 1) for a in range(n - 1)]
    leftward = [(a, a - 1) for a in range(1, n)]
    lefts, rights = [], []
    from_left, from_right = x, x
    for _ in range(1, n):
        from_left = lax.ppermute(from_left, axis, rightward)
        from_right = lax.ppermute(from_right, axis, leftward)
        lefts.append(from_left)
        rights.append(from_right)
    line = jnp.concatenate(lefts[::-1] + [x] + rights)
    return lax.dynamic_slice_in_dim(line, (n - 1 - me) * x.shape[0], n * x.shape[0])


def packed_partials(lam, int_kept, pick, order, valid, col_of, col_tiles, cap):
    received = line_gather(int_kept[:cap], "occ")
    row_tiles, cd_width = pick.shape
    edge = int_kept.shape[1]
    lam3 = lam.reshape(row_tiles, edge, cd_width)
    lam_kept = jnp.sum(jnp.where(pick[:, None, :], lam3, jnp.zeros((), lam.dtype)), axis=0)
    lam_kept = lam_kept.reshape(edge, cd_width // edge, edge).transpose(1, 0, 2)
    q = order[:, :cap].reshape(-1)
    t = col_of[:, :cap].reshape(-1)
    ok = valid[:, :cap].reshape(-1)
    lam_tiles = jnp.where(ok[:, None, None], lam_kept[q], jnp.zeros((), lam_kept.dtype))
    products = jnp.einsum(
        "srm,smc->src", lam_tiles, received, preferred_element_type=jnp.float32
    )
    onehot = (t[None, :] == jnp.arange(col_tiles)[:, None]) & ok[None, :]
    return jnp.einsum(
        "ts,src->trc", onehot.astype(jnp.float32), products, precision=lax.Precision.HIGHEST
    )


def on_device(lam, integrals, occ_sym, cd_sym, ab_sym):
    row_tiles = occ_sym.shape[0]
    cd_tiles = cd_sym.shape[0]
    tile_edge = lam.shape[0] // row_tiles
    col_tiles = ab_sym.shape[0]
    own_cols = integrals.shape[1] // tile_edge
    peers = col_tiles // own_cols
    row_of = jnp.argmax(occ_sym[None, :] == ab_sym[:, None], axis=1)
    kept = cd_sym[:, None] == ab_sym[None, :]
    kept = kept.reshape(cd_tiles, peers, own_cols).transpose(1, 0, 2)
    need = jnp.max(jnp.sum(kept, axis=(1, 2)))
    dense = cd_tiles * own_cols
    flat = kept.reshape(peers, dense)
    rank = jnp.cumsum(flat, axis=1) - 1
    hit = flat[:, None, :] & (rank[:, None, :] == jnp.arange(dense)[None, :, None])
    slot = jnp.sum(hit * jnp.arange(dense), axis=2)
    valid = jnp.any(hit, axis=2)
    order = slot // own_cols
    col_of = jnp.arange(peers)[:, None] * own_cols + slot % own_cols
    me = lax.axis_index("occ")
    blocks = integrals.reshape(cd_tiles, tile_edge, own_cols * tile_edge)[order[me]]
    int_kept = blocks[:, :, :tile_edge]
    for col in range(1, own_cols):
        pick = (slot[me] % own_cols == col)[:, None, None]
        int_kept = jnp.where(pick, blocks[:, :, col * tile_edge:(col + 1) * tile_edge], int_kept)
    row_for_q = jnp.argmax(occ_sym[:, None] == cd_sym[None, :], axis=0)
    pick = jnp.repeat(row_for_q[None, :] == jnp.arange(row_tiles)[:, None], tile_edge, axis=1)
    caps = sorted({max(1, dense // 4), max(1, dense // 3), max(1, dense // 2), dense})
    branch = sum((need > cap).astype(jnp.int32) for cap in caps[:-1])
    partial_sum = lax.switch(
        branch,
        [
            lambda l, i, cap=cap: packed_partials(l, i, pick, order, valid, col_of, col_tiles, cap)
            for cap in caps
        ],
        lam,
        int_kept,
    )
    summed = halving_reduce_scatter(partial_sum, "vir")
    own_row = row_of[lax.axis_index("vir")]
    keep = (jnp.arange(row_tiles) == own_row)[:, None, None]
    out = jnp.where(keep, summed.astype(jnp.bfloat16)[None], jnp.zeros((), jnp.bfloat16))
    return out.reshape(row_tiles * tile_edge, summed.shape[1])


def solution(mesh):
    in_specs = (P("occ", "vir"), P("vir", "occ"), P("occ"), P("vir"), P())
    out_specs = P("occ", "vir")
    return jax.shard_map(
        on_device, mesh=mesh, in_specs=in_specs, out_specs=out_specs, check_vma=False
    )
```

```python
import jax
import jax.numpy as jnp
from jax import lax
from jax.sharding import PartitionSpec as P


def halving_reduce_scatter(parts, axis):
    n = lax.axis_size(axis)
    me = lax.axis_index(axis)
    step = 1
    while step < n:
        bit = (me // step) % 2
        pairs = parts.reshape(parts.shape[0] // 2, 2, *parts.shape[1:])
        keep = lax.dynamic_index_in_dim(pairs, bit, axis=1, keepdims=False)
        send = lax.dynamic_index_in_dim(pairs, 1 - bit, axis=1, keepdims=False)
        perm = [(j, j ^ step) for j in range(n)]
        parts = keep + lax.ppermute(send, axis, perm)
        step *= 2
    return parts[0]


def doubling_max(value, axis):
    n = lax.axis_size(axis)
    step = 1
    while step < n:
        value = jnp.maximum(value, lax.ppermute(value, axis, [(j, j ^ step) for j in range(n)]))
        step *= 2
    return value


def line_gather(x, axis):
    n = lax.axis_size(axis)
    me = lax.axis_index(axis)
    rightward = [(a, a + 1) for a in range(n - 1)]
    leftward = [(a, a - 1) for a in range(1, n)]
    lefts, rights = [], []
    from_left, from_right = x, x
    for _ in range(1, n):
        from_left = lax.ppermute(from_left, axis, rightward)
        from_right = lax.ppermute(from_right, axis, leftward)
        lefts.append(from_left)
        rights.append(from_right)
    line = jnp.concatenate(lefts[::-1] + [x] + rights)
    return lax.dynamic_slice_in_dim(line, (n - 1 - me) * x.shape[0], n * x.shape[0])


def packed_partials(lam_kept, int_kept, order, valid, col_of, col_tiles, cap):
    received = line_gather(int_kept[:cap], "occ")
    q = order[:, :cap].reshape(-1)
    t = col_of[:, :cap].reshape(-1)
    ok = valid[:, :cap].reshape(-1)
    lam_tiles = jnp.where(ok[:, None, None], lam_kept[q], jnp.zeros((), lam_kept.dtype))
    products = jnp.einsum(
        "srm,smc->src", lam_tiles, received, preferred_element_type=jnp.float32
    )
    onehot = (t[None, :] == jnp.arange(col_tiles)[:, None]) & ok[None, :]
    return jnp.einsum(
        "ts,src->trc", onehot.astype(jnp.float32), products, precision=lax.Precision.HIGHEST
    )


def on_device(lam, integrals, occ_sym, cd_sym, ab_sym):
    row_tiles = occ_sym.shape[0]
    cd_tiles = cd_sym.shape[0]
    tile_edge = lam.shape[0] // row_tiles
    col_tiles = ab_sym.shape[0]
    own_cols = integrals.shape[1] // tile_edge
    peers = col_tiles // own_cols
    row_of = jnp.argmax(occ_sym[None, :] == ab_sym[:, None], axis=1)
    kept = cd_sym[:, None] == ab_sym[None, :]
    kept = kept.reshape(cd_tiles, peers, own_cols).transpose(1, 0, 2)
    need = jnp.max(jnp.sum(kept, axis=(1, 2)))
    dense = cd_tiles * own_cols
    flat = kept.reshape(peers, dense)
    rank = jnp.cumsum(flat, axis=1) - 1
    hit = flat[:, None, :] & (rank[:, None, :] == jnp.arange(dense)[None, :, None])
    slot = jnp.sum(hit * jnp.arange(dense), axis=2)
    valid = jnp.any(hit, axis=2)
    order = slot // own_cols
    col_of = jnp.arange(peers)[:, None] * own_cols + slot % own_cols
    me = lax.axis_index("occ")
    blocks = integrals.reshape(cd_tiles, tile_edge, own_cols * tile_edge)[order[me]]
    int_kept = blocks[:, :, :tile_edge]
    for col in range(1, own_cols):
        pick = (slot[me] % own_cols == col)[:, None, None]
        int_kept = jnp.where(pick, blocks[:, :, col * tile_edge:(col + 1) * tile_edge], int_kept)
    row_for_q = jnp.argmax(occ_sym[:, None] == cd_sym[None, :], axis=0)
    lam3 = lam.reshape(row_tiles, tile_edge, cd_tiles * tile_edge)
    pick = jnp.repeat(row_for_q[None, :] == jnp.arange(row_tiles)[:, None], tile_edge, axis=1)
    lam_kept = jnp.sum(jnp.where(pick[:, None, :], lam3, jnp.zeros((), lam.dtype)), axis=0)
    lam_kept = lam_kept.reshape(tile_edge, cd_tiles, tile_edge).transpose(1, 0, 2)
    caps = sorted({max(1, dense // 3), max(1, dense // 2), dense})
    branch = sum((need > cap).astype(jnp.int32) for cap in caps[:-1])
    partial_sum = lax.switch(
        branch,
        [
            lambda l, i, cap=cap: packed_partials(l, i, order, valid, col_of, col_tiles, cap)
            for cap in caps
        ],
        lam_kept,
        int_kept,
    )
    pieces = lax.all_to_all(partial_sum, "vir", split_axis=0, concat_axis=0, tiled=True)
    summed = jnp.sum(pieces, axis=0)
    own_row = row_of[lax.axis_index("vir")]
    keep = (jnp.arange(row_tiles) == own_row)[:, None, None]
    out = jnp.where(keep, summed.astype(jnp.bfloat16)[None], jnp.zeros((), jnp.bfloat16))
    return out.reshape(row_tiles * tile_edge, summed.shape[1])


def solution(mesh):
    in_specs = (P("occ", "vir"), P("vir", "occ"), P("occ"), P("vir"), P())
    out_specs = P("occ", "vir")
    return jax.shard_map(
        on_device, mesh=mesh, in_specs=in_specs, out_specs=out_specs, check_vma=False
    )
```

```python
import jax
import jax.numpy as jnp
from jax import lax
from jax.sharding import PartitionSpec as P


def halving_reduce_scatter(parts, axis):
    n = lax.axis_size(axis)
    me = lax.axis_index(axis)
    step = 1
    while step < n:
        bit = (me // step) % 2
        pairs = parts.reshape(parts.shape[0] // 2, 2, *parts.shape[1:])
        keep = lax.dynamic_index_in_dim(pairs, bit, axis=1, keepdims=False)
        send = lax.dynamic_index_in_dim(pairs, 1 - bit, axis=1, keepdims=False)
        perm = [(j, j ^ step) for j in range(n)]
        parts = keep + lax.ppermute(send, axis, perm)
        step *= 2
    return parts[0]


def doubling_max(value, axis):
    n = lax.axis_size(axis)
    step = 1
    while step < n:
        value = jnp.maximum(value, lax.ppermute(value, axis, [(j, j ^ step) for j in range(n)]))
        step *= 2
    return value


def line_gather(x, axis):
    n = lax.axis_size(axis)
    me = lax.axis_index(axis)
    rightward = [(a, a + 1) for a in range(n - 1)]
    leftward = [(a, a - 1) for a in range(1, n)]
    lefts, rights = [], []
    from_left, from_right = x, x
    for _ in range(1, n):
        from_left = lax.ppermute(from_left, axis, rightward)
        from_right = lax.ppermute(from_right, axis, leftward)
        lefts.append(from_left)
        rights.append(from_right)
    line = jnp.concatenate(lefts[::-1] + [x] + rights)
    return lax.dynamic_slice_in_dim(line, (n - 1 - me) * x.shape[0], n * x.shape[0])


def packed_partials(lam_kept, int_kept, order, valid, col_of, col_tiles, cap):
    received = line_gather(int_kept[:cap], "occ")
    q = order[:, :cap].reshape(-1)
    t = col_of[:, :cap].reshape(-1)
    ok = valid[:, :cap].reshape(-1)
    lam_tiles = jnp.where(ok[:, None, None], lam_kept[q], jnp.zeros((), lam_kept.dtype))
    products = jnp.einsum(
        "srm,smc->src", lam_tiles, received, preferred_element_type=jnp.float32
    )
    onehot = (t[None, :] == jnp.arange(col_tiles)[:, None]) & ok[None, :]
    return jnp.einsum(
        "ts,src->trc", onehot.astype(jnp.float32), products, precision=lax.Precision.HIGHEST
    )


def on_device(lam, integrals, occ_sym, cd_sym, ab_sym):
    row_tiles = occ_sym.shape[0]
    cd_tiles = cd_sym.shape[0]
    tile_edge = lam.shape[0] // row_tiles
    col_tiles = ab_sym.shape[0]
    own_cols = integrals.shape[1] // tile_edge
    peers = col_tiles // own_cols
    row_of = jnp.argmax(occ_sym[None, :] == ab_sym[:, None], axis=1)
    kept = cd_sym[:, None] == ab_sym[None, :]
    kept = kept.reshape(cd_tiles, peers, own_cols).transpose(1, 0, 2)
    need = jnp.max(jnp.sum(kept, axis=(1, 2)))
    dense = cd_tiles * own_cols
    flat = kept.reshape(peers, dense)
    rank = jnp.cumsum(flat, axis=1) - 1
    hit = flat[:, None, :] & (rank[:, None, :] == jnp.arange(dense)[None, :, None])
    slot = jnp.sum(hit * jnp.arange(dense), axis=2)
    valid = jnp.any(hit, axis=2)
    order = slot // own_cols
    col_of = jnp.arange(peers)[:, None] * own_cols + slot % own_cols
    me = lax.axis_index("occ")
    blocks = integrals.reshape(cd_tiles, tile_edge, own_cols * tile_edge)[order[me]]
    int_kept = blocks[:, :, :tile_edge]
    for col in range(1, own_cols):
        pick = (slot[me] % own_cols == col)[:, None, None]
        int_kept = jnp.where(pick, blocks[:, :, col * tile_edge:(col + 1) * tile_edge], int_kept)
    row_for_q = jnp.argmax(occ_sym[:, None] == cd_sym[None, :], axis=0)
    lam3 = lam.reshape(row_tiles, tile_edge, cd_tiles * tile_edge)
    pick = jnp.repeat(row_for_q[None, :] == jnp.arange(row_tiles)[:, None], tile_edge, axis=1)
    lam_kept = jnp.sum(jnp.where(pick[:, None, :], lam3, jnp.zeros((), lam.dtype)), axis=0)
    lam_kept = lam_kept.reshape(tile_edge, cd_tiles, tile_edge).transpose(1, 0, 2)
    caps = sorted({max(1, dense // 4), max(1, dense // 3), max(1, dense // 2), dense})
    branch = sum((need > cap).astype(jnp.int32) for cap in caps[:-1])
    partial_sum = lax.switch(
        branch,
        [
            lambda l, i, cap=cap: packed_partials(l, i, order, valid, col_of, col_tiles, cap)
            for cap in caps
        ],
        lam_kept,
        int_kept,
    )
    summed = halving_reduce_scatter(partial_sum, "vir")
    own_row = row_of[lax.axis_index("vir")]
    keep = (jnp.arange(row_tiles) == own_row)[:, None, None]
    out = jnp.where(keep, summed.astype(jnp.bfloat16)[None], jnp.zeros((), jnp.bfloat16))
    return out.reshape(row_tiles * tile_edge, summed.shape[1])


def solution(mesh):
    in_specs = (P("occ", "vir"), P("vir", "occ"), P("occ"), P("vir"), P())
    out_specs = P("occ", "vir")
    return jax.shard_map(
        on_device, mesh=mesh, in_specs=in_specs, out_specs=out_specs, check_vma=False
    )
```

```python
import jax
import jax.numpy as jnp
from jax import lax
from jax.sharding import PartitionSpec as P


def halving_reduce_scatter(parts, axis):
    n = lax.axis_size(axis)
    me = lax.axis_index(axis)
    step = 1
    while step < n:
        bit = (me // step) % 2
        pairs = parts.reshape(parts.shape[0] // 2, 2, *parts.shape[1:])
        keep = lax.dynamic_index_in_dim(pairs, bit, axis=1, keepdims=False)
        send = lax.dynamic_index_in_dim(pairs, 1 - bit, axis=1, keepdims=False)
        perm = [(j, j ^ step) for j in range(n)]
        parts = keep + lax.ppermute(send, axis, perm)
        step *= 2
    return parts[0]


def doubling_max(value, axis):
    n = lax.axis_size(axis)
    step = 1
    while step < n:
        value = jnp.maximum(value, lax.ppermute(value, axis, [(j, j ^ step) for j in range(n)]))
        step *= 2
    return value


def line_gather(x, axis):
    n = lax.axis_size(axis)
    me = lax.axis_index(axis)
    rightward = [(a, a + 1) for a in range(n - 1)]
    leftward = [(a, a - 1) for a in range(1, n)]
    lefts, rights = [], []
    from_left, from_right = x, x
    for _ in range(1, n):
        from_left = lax.ppermute(from_left, axis, rightward)
        from_right = lax.ppermute(from_right, axis, leftward)
        lefts.append(from_left)
        rights.append(from_right)
    line = jnp.concatenate(lefts[::-1] + [x] + rights)
    return lax.dynamic_slice_in_dim(line, (n - 1 - me) * x.shape[0], n * x.shape[0])


def packed_partials(lam_kept, int_kept, order, valid, col_of, col_tiles, cap):
    halves = [int_kept[:cap // 2], int_kept[cap // 2:cap]] if cap > 1 else [int_kept[:cap]]
    peers = order.shape[0]
    received = jnp.concatenate(
        [line_gather(h, "occ").reshape(peers, h.shape[0], *h.shape[1:]) for h in halves], axis=1
    ).reshape(peers * cap, *int_kept.shape[1:])
    q = order[:, :cap].reshape(-1)
    t = col_of[:, :cap].reshape(-1)
    ok = valid[:, :cap].reshape(-1)
    lam_tiles = jnp.where(ok[:, None, None], lam_kept[q], jnp.zeros((), lam_kept.dtype))
    products = jnp.einsum(
        "srm,smc->src", lam_tiles, received, preferred_element_type=jnp.float32
    )
    onehot = (t[None, :] == jnp.arange(col_tiles)[:, None]) & ok[None, :]
    return jnp.einsum(
        "ts,src->trc", onehot.astype(jnp.float32), products, precision=lax.Precision.HIGHEST
    )


def on_device(lam, integrals, occ_sym, cd_sym, ab_sym):
    row_tiles = occ_sym.shape[0]
    cd_tiles = cd_sym.shape[0]
    tile_edge = lam.shape[0] // row_tiles
    col_tiles = ab_sym.shape[0]
    own_cols = integrals.shape[1] // tile_edge
    peers = col_tiles // own_cols
    row_of = jnp.argmax(occ_sym[None, :] == ab_sym[:, None], axis=1)
    kept = cd_sym[:, None] == ab_sym[None, :]
    kept = kept.reshape(cd_tiles, peers, own_cols).transpose(1, 0, 2)
    need = jnp.max(jnp.sum(kept, axis=(1, 2)))
    dense = cd_tiles * own_cols
    flat = kept.reshape(peers, dense)
    rank = jnp.cumsum(flat, axis=1) - 1
    hit = flat[:, None, :] & (rank[:, None, :] == jnp.arange(dense)[None, :, None])
    slot = jnp.sum(hit * jnp.arange(dense), axis=2)
    valid = jnp.any(hit, axis=2)
    order = slot // own_cols
    col_of = jnp.arange(peers)[:, None] * own_cols + slot % own_cols
    me = lax.axis_index("occ")
    blocks = integrals.reshape(cd_tiles, tile_edge, own_cols * tile_edge)[order[me]]
    int_kept = blocks[:, :, :tile_edge]
    for col in range(1, own_cols):
        pick = (slot[me] % own_cols == col)[:, None, None]
        int_kept = jnp.where(pick, blocks[:, :, col * tile_edge:(col + 1) * tile_edge], int_kept)
    row_for_q = jnp.argmax(occ_sym[:, None] == cd_sym[None, :], axis=0)
    lam3 = lam.reshape(row_tiles, tile_edge, cd_tiles * tile_edge)
    pick = jnp.repeat(row_for_q[None, :] == jnp.arange(row_tiles)[:, None], tile_edge, axis=1)
    lam_kept = jnp.sum(jnp.where(pick[:, None, :], lam3, jnp.zeros((), lam.dtype)), axis=0)
    lam_kept = lam_kept.reshape(tile_edge, cd_tiles, tile_edge).transpose(1, 0, 2)
    caps = sorted({max(1, dense // 3), max(1, dense // 2), dense})
    branch = sum((need > cap).astype(jnp.int32) for cap in caps[:-1])
    partial_sum = lax.switch(
        branch,
        [
            lambda l, i, cap=cap: packed_partials(l, i, order, valid, col_of, col_tiles, cap)
            for cap in caps
        ],
        lam_kept,
        int_kept,
    )
    summed = halving_reduce_scatter(partial_sum, "vir")
    own_row = row_of[lax.axis_index("vir")]
    keep = (jnp.arange(row_tiles) == own_row)[:, None, None]
    out = jnp.where(keep, summed.astype(jnp.bfloat16)[None], jnp.zeros((), jnp.bfloat16))
    return out.reshape(row_tiles * tile_edge, summed.shape[1])


def solution(mesh):
    in_specs = (P("occ", "vir"), P("vir", "occ"), P("occ"), P("vir"), P())
    out_specs = P("occ", "vir")
    return jax.shard_map(
        on_device, mesh=mesh, in_specs=in_specs, out_specs=out_specs, check_vma=False
    )
```

```python
import jax
import jax.numpy as jnp
from jax import lax
from jax.sharding import PartitionSpec as P


def halving_reduce_scatter(parts, axis):
    n = lax.axis_size(axis)
    me = lax.axis_index(axis)
    step = 1
    while step < n:
        bit = (me // step) % 2
        pairs = parts.reshape(parts.shape[0] // 2, 2, *parts.shape[1:])
        keep = lax.dynamic_index_in_dim(pairs, bit, axis=1, keepdims=False)
        send = lax.dynamic_index_in_dim(pairs, 1 - bit, axis=1, keepdims=False)
        perm = [(j, j ^ step) for j in range(n)]
        parts = keep + lax.ppermute(send, axis, perm)
        step *= 2
    return parts[0]


def doubling_max(value, axis):
    n = lax.axis_size(axis)
    step = 1
    while step < n:
        value = jnp.maximum(value, lax.ppermute(value, axis, [(j, j ^ step) for j in range(n)]))
        step *= 2
    return value


def line_gather(x, axis):
    n = lax.axis_size(axis)
    me = lax.axis_index(axis)
    rightward = [(a, a + 1) for a in range(n - 1)]
    leftward = [(a, a - 1) for a in range(1, n)]
    lefts, rights = [], []
    from_left, from_right = x, x
    for _ in range(1, n):
        from_left = lax.ppermute(from_left, axis, rightward)
        from_right = lax.ppermute(from_right, axis, leftward)
        lefts.append(from_left)
        rights.append(from_right)
    line = jnp.concatenate(lefts[::-1] + [x] + rights)
    return lax.dynamic_slice_in_dim(line, (n - 1 - me) * x.shape[0], n * x.shape[0])


def packed_partials(lam_kept, int_kept, order, valid, col_of, col_tiles, cap):
    received = line_gather(int_kept[:cap], "occ")
    q = order[:, :cap].reshape(-1)
    t = col_of[:, :cap].reshape(-1)
    ok = valid[:, :cap].reshape(-1)
    lam_tiles = jnp.where(ok[:, None, None], lam_kept[q], jnp.zeros((), lam_kept.dtype))
    products = jnp.einsum(
        "srm,smc->src", lam_tiles, received, preferred_element_type=jnp.float32
    )
    peers = order.shape[0]
    own_cols = col_tiles // peers
    c = (t % own_cols).reshape(peers, 1, cap)
    mine = (c == jnp.arange(own_cols)[None, :, None]) & ok.reshape(peers, 1, cap)
    products = products.reshape(peers, 1, cap, *products.shape[1:])
    partial = jnp.sum(jnp.where(mine[..., None, None], products, 0.0), axis=2)
    return partial.reshape(col_tiles, *partial.shape[2:])


def on_device(lam, integrals, occ_sym, cd_sym, ab_sym):
    row_tiles = occ_sym.shape[0]
    cd_tiles = cd_sym.shape[0]
    tile_edge = lam.shape[0] // row_tiles
    col_tiles = ab_sym.shape[0]
    own_cols = integrals.shape[1] // tile_edge
    peers = col_tiles // own_cols
    row_of = jnp.argmax(occ_sym[None, :] == ab_sym[:, None], axis=1)
    kept = cd_sym[:, None] == ab_sym[None, :]
    kept = kept.reshape(cd_tiles, peers, own_cols).transpose(1, 0, 2)
    need = jnp.max(jnp.sum(kept, axis=(1, 2)))
    dense = cd_tiles * own_cols
    flat = kept.reshape(peers, dense)
    rank = jnp.cumsum(flat, axis=1) - 1
    hit = flat[:, None, :] & (rank[:, None, :] == jnp.arange(dense)[None, :, None])
    slot = jnp.sum(hit * jnp.arange(dense), axis=2)
    valid = jnp.any(hit, axis=2)
    order = slot // own_cols
    col_of = jnp.arange(peers)[:, None] * own_cols + slot % own_cols
    me = lax.axis_index("occ")
    blocks = integrals.reshape(cd_tiles, tile_edge, own_cols * tile_edge)[order[me]]
    int_kept = blocks[:, :, :tile_edge]
    for col in range(1, own_cols):
        pick = (slot[me] % own_cols == col)[:, None, None]
        int_kept = jnp.where(pick, blocks[:, :, col * tile_edge:(col + 1) * tile_edge], int_kept)
    row_for_q = jnp.argmax(occ_sym[:, None] == cd_sym[None, :], axis=0)
    lam3 = lam.reshape(row_tiles, tile_edge, cd_tiles * tile_edge)
    pick = jnp.repeat(row_for_q[None, :] == jnp.arange(row_tiles)[:, None], tile_edge, axis=1)
    lam_kept = jnp.sum(jnp.where(pick[:, None, :], lam3, jnp.zeros((), lam.dtype)), axis=0)
    lam_kept = lam_kept.reshape(tile_edge, cd_tiles, tile_edge).transpose(1, 0, 2)
    caps = sorted({max(1, dense // 3), max(1, dense // 2), dense})
    branch = sum((need > cap).astype(jnp.int32) for cap in caps[:-1])
    partial_sum = lax.switch(
        branch,
        [
            lambda l, i, cap=cap: packed_partials(l, i, order, valid, col_of, col_tiles, cap)
            for cap in caps
        ],
        lam_kept,
        int_kept,
    )
    summed = halving_reduce_scatter(partial_sum, "vir")
    own_row = row_of[lax.axis_index("vir")]
    keep = (jnp.arange(row_tiles) == own_row)[:, None, None]
    out = jnp.where(keep, summed.astype(jnp.bfloat16)[None], jnp.zeros((), jnp.bfloat16))
    return out.reshape(row_tiles * tile_edge, summed.shape[1])


def solution(mesh):
    in_specs = (P("occ", "vir"), P("vir", "occ"), P("occ"), P("vir"), P())
    out_specs = P("occ", "vir")
    return jax.shard_map(
        on_device, mesh=mesh, in_specs=in_specs, out_specs=out_specs, check_vma=False
    )
```

```python
import jax
import jax.numpy as jnp
from jax import lax
from jax.sharding import PartitionSpec as P


def halving_reduce_scatter(parts, axis):
    n = lax.axis_size(axis)
    me = lax.axis_index(axis)
    step = 1
    while step < n:
        bit = (me // step) % 2
        pairs = parts.reshape(parts.shape[0] // 2, 2, *parts.shape[1:])
        keep = lax.dynamic_index_in_dim(pairs, bit, axis=1, keepdims=False)
        send = lax.dynamic_index_in_dim(pairs, 1 - bit, axis=1, keepdims=False)
        perm = [(j, j ^ step) for j in range(n)]
        parts = keep + lax.ppermute(send, axis, perm)
        step *= 2
    return parts[0]


def doubling_max(value, axis):
    n = lax.axis_size(axis)
    step = 1
    while step < n:
        value = jnp.maximum(value, lax.ppermute(value, axis, [(j, j ^ step) for j in range(n)]))
        step *= 2
    return value


def line_gather(x, axis):
    n = lax.axis_size(axis)
    me = lax.axis_index(axis)
    rightward = [(a, a + 1) for a in range(n - 1)]
    leftward = [(a, a - 1) for a in range(1, n)]
    lefts, rights = [], []
    from_left, from_right = x, x
    for _ in range(1, n):
        from_left = lax.ppermute(from_left, axis, rightward)
        from_right = lax.ppermute(from_right, axis, leftward)
        lefts.append(from_left)
        rights.append(from_right)
    line = jnp.concatenate(lefts[::-1] + [x] + rights)
    return lax.dynamic_slice_in_dim(line, (n - 1 - me) * x.shape[0], n * x.shape[0])


def packed_partials(lam_kept, int_kept, order, valid, col_of, col_tiles, cap):
    received = line_gather(int_kept[:cap], "occ")
    q = order[:, :cap].reshape(-1)
    t = col_of[:, :cap].reshape(-1)
    ok = valid[:, :cap].reshape(-1)
    lam_tiles = jnp.where(ok[:, None, None], lam_kept[q], jnp.zeros((), lam_kept.dtype))
    products = jnp.einsum(
        "srm,smc->src", lam_tiles, received, preferred_element_type=jnp.float32
    )
    peers = order.shape[0]
    own_cols = col_tiles // peers
    c = (t % own_cols).reshape(peers, 1, cap)
    mine = (c == jnp.arange(own_cols)[None, :, None]) & ok.reshape(peers, 1, cap)
    products = products.reshape(peers, 1, cap, *products.shape[1:])
    partial = jnp.sum(jnp.where(mine[..., None, None], products, 0.0), axis=2)
    return partial.reshape(col_tiles, *partial.shape[2:])


def on_device(lam, integrals, occ_sym, cd_sym, ab_sym):
    row_tiles = occ_sym.shape[0]
    cd_tiles = cd_sym.shape[0]
    tile_edge = lam.shape[0] // row_tiles
    col_tiles = ab_sym.shape[0]
    own_cols = integrals.shape[1] // tile_edge
    peers = col_tiles // own_cols
    row_of = jnp.argmax(occ_sym[None, :] == ab_sym[:, None], axis=1)
    kept = cd_sym[:, None] == ab_sym[None, :]
    kept = kept.reshape(cd_tiles, peers, own_cols).transpose(1, 0, 2)
    need = jnp.max(jnp.sum(kept, axis=(1, 2)))
    dense = cd_tiles * own_cols
    flat = kept.reshape(peers, dense)
    rank = jnp.cumsum(flat, axis=1) - 1
    hit = flat[:, None, :] & (rank[:, None, :] == jnp.arange(dense)[None, :, None])
    slot = jnp.sum(hit * jnp.arange(dense), axis=2)
    valid = jnp.any(hit, axis=2)
    order = slot // own_cols
    col_of = jnp.arange(peers)[:, None] * own_cols + slot % own_cols
    me = lax.axis_index("occ")
    blocks = integrals.reshape(cd_tiles, tile_edge, own_cols * tile_edge)[order[me]]
    int_kept = blocks[:, :, :tile_edge]
    for col in range(1, own_cols):
        pick = (slot[me] % own_cols == col)[:, None, None]
        int_kept = jnp.where(pick, blocks[:, :, col * tile_edge:(col + 1) * tile_edge], int_kept)
    row_for_q = jnp.argmax(occ_sym[:, None] == cd_sym[None, :], axis=0)
    lam3 = lam.reshape(row_tiles, tile_edge, cd_tiles * tile_edge)
    pick = jnp.repeat(row_for_q[None, :] == jnp.arange(row_tiles)[:, None], tile_edge, axis=1)
    lam_kept = jnp.sum(jnp.where(pick[:, None, :], lam3, jnp.zeros((), lam.dtype)), axis=0)
    lam_kept = lam_kept.reshape(tile_edge, cd_tiles, tile_edge).transpose(1, 0, 2)
    caps = sorted({max(1, dense // 4), max(1, dense // 3), max(1, dense // 2), dense})
    branch = sum((need > cap).astype(jnp.int32) for cap in caps[:-1])
    partial_sum = lax.switch(
        branch,
        [
            lambda l, i, cap=cap: packed_partials(l, i, order, valid, col_of, col_tiles, cap)
            for cap in caps
        ],
        lam_kept,
        int_kept,
    )
    summed = halving_reduce_scatter(partial_sum, "vir")
    own_row = row_of[lax.axis_index("vir")]
    keep = (jnp.arange(row_tiles) == own_row)[:, None, None]
    out = jnp.where(keep, summed.astype(jnp.bfloat16)[None], jnp.zeros((), jnp.bfloat16))
    return out.reshape(row_tiles * tile_edge, summed.shape[1])


def solution(mesh):
    in_specs = (P("occ", "vir"), P("vir", "occ"), P("occ"), P("vir"), P())
    out_specs = P("occ", "vir")
    return jax.shard_map(
        on_device, mesh=mesh, in_specs=in_specs, out_specs=out_specs, check_vma=False
    )
```

```python
import jax
import jax.numpy as jnp
from jax import lax
from jax.sharding import PartitionSpec as P


def halving_reduce_scatter(parts, axis):
    n = lax.axis_size(axis)
    me = lax.axis_index(axis)
    step = 1
    while step < n:
        bit = (me // step) % 2
        pairs = parts.reshape(parts.shape[0] // 2, 2, *parts.shape[1:])
        keep = lax.dynamic_index_in_dim(pairs, bit, axis=1, keepdims=False)
        send = lax.dynamic_index_in_dim(pairs, 1 - bit, axis=1, keepdims=False)
        perm = [(j, j ^ step) for j in range(n)]
        parts = keep + lax.ppermute(send, axis, perm)
        step *= 2
    return parts[0]


def doubling_max(value, axis):
    n = lax.axis_size(axis)
    step = 1
    while step < n:
        value = jnp.maximum(value, lax.ppermute(value, axis, [(j, j ^ step) for j in range(n)]))
        step *= 2
    return value


def line_gather(x, axis):
    n = lax.axis_size(axis)
    me = lax.axis_index(axis)
    rightward = [(a, a + 1) for a in range(n - 1)]
    leftward = [(a, a - 1) for a in range(1, n)]
    lefts, rights = [], []
    from_left, from_right = x, x
    for _ in range(1, n):
        from_left = lax.ppermute(from_left, axis, rightward)
        from_right = lax.ppermute(from_right, axis, leftward)
        lefts.append(from_left)
        rights.append(from_right)
    line = jnp.concatenate(lefts[::-1] + [x] + rights)
    return lax.dynamic_slice_in_dim(line, (n - 1 - me) * x.shape[0], n * x.shape[0])


def packed_partials(lam_kept, int_kept, order, valid, col_of, col_tiles, cap):
    received = line_gather(int_kept[:cap], "occ")
    q = order[:, :cap].reshape(-1)
    t = col_of[:, :cap].reshape(-1)
    ok = valid[:, :cap].reshape(-1)
    products = jnp.einsum(
        "srm,smc->src", lam_kept[q], received, preferred_element_type=jnp.float32
    )
    peers = order.shape[0]
    own_cols = col_tiles // peers
    c = (t % own_cols).reshape(peers, 1, cap)
    mine = (c == jnp.arange(own_cols)[None, :, None]) & ok.reshape(peers, 1, cap)
    products = products.reshape(peers, 1, cap, *products.shape[1:])
    partial = jnp.sum(jnp.where(mine[..., None, None], products, 0.0), axis=2)
    return partial.reshape(col_tiles, *partial.shape[2:])


def on_device(lam, integrals, occ_sym, cd_sym, ab_sym):
    row_tiles = occ_sym.shape[0]
    cd_tiles = cd_sym.shape[0]
    tile_edge = lam.shape[0] // row_tiles
    col_tiles = ab_sym.shape[0]
    own_cols = integrals.shape[1] // tile_edge
    peers = col_tiles // own_cols
    row_of = jnp.argmax(occ_sym[None, :] == ab_sym[:, None], axis=1)
    kept = cd_sym[:, None] == ab_sym[None, :]
    kept = kept.reshape(cd_tiles, peers, own_cols).transpose(1, 0, 2)
    need = jnp.max(jnp.sum(kept, axis=(1, 2)))
    dense = cd_tiles * own_cols
    flat = kept.reshape(peers, dense)
    rank = jnp.cumsum(flat, axis=1) - 1
    hit = flat[:, None, :] & (rank[:, None, :] == jnp.arange(dense)[None, :, None])
    slot = jnp.sum(hit * jnp.arange(dense), axis=2)
    valid = jnp.any(hit, axis=2)
    order = slot // own_cols
    col_of = jnp.arange(peers)[:, None] * own_cols + slot % own_cols
    me = lax.axis_index("occ")
    blocks = integrals.reshape(cd_tiles, tile_edge, own_cols * tile_edge)[order[me]]
    int_kept = blocks[:, :, :tile_edge]
    for col in range(1, own_cols):
        pick = (slot[me] % own_cols == col)[:, None, None]
        int_kept = jnp.where(pick, blocks[:, :, col * tile_edge:(col + 1) * tile_edge], int_kept)
    row_for_q = jnp.argmax(occ_sym[:, None] == cd_sym[None, :], axis=0)
    lam3 = lam.reshape(row_tiles, tile_edge, cd_tiles * tile_edge)
    pick = jnp.repeat(row_for_q[None, :] == jnp.arange(row_tiles)[:, None], tile_edge, axis=1)
    lam_kept = jnp.sum(jnp.where(pick[:, None, :], lam3, jnp.zeros((), lam.dtype)), axis=0)
    lam_kept = lam_kept.reshape(tile_edge, cd_tiles, tile_edge).transpose(1, 0, 2)
    caps = sorted({max(1, dense // 4), max(1, dense // 3), max(1, dense // 2), dense})
    branch = sum((need > cap).astype(jnp.int32) for cap in caps[:-1])
    partial_sum = lax.switch(
        branch,
        [
            lambda l, i, cap=cap: packed_partials(l, i, order, valid, col_of, col_tiles, cap)
            for cap in caps
        ],
        lam_kept,
        int_kept,
    )
    summed = halving_reduce_scatter(partial_sum, "vir")
    own_row = row_of[lax.axis_index("vir")]
    keep = (jnp.arange(row_tiles) == own_row)[:, None, None]
    out = jnp.where(keep, summed.astype(jnp.bfloat16)[None], jnp.zeros((), jnp.bfloat16))
    return out.reshape(row_tiles * tile_edge, summed.shape[1])


def solution(mesh):
    in_specs = (P("occ", "vir"), P("vir", "occ"), P("occ"), P("vir"), P())
    out_specs = P("occ", "vir")
    return jax.shard_map(
        on_device, mesh=mesh, in_specs=in_specs, out_specs=out_specs, check_vma=False
    )
```
